256 devices in a mesh: row: 8 (over z), col: 32 (over x, y, core).
Axes of the slice: x: 4, y: 4, z: 8, core: 2. Of those that a mesh axis runs over, the one named last changes fastest.
Arguments:
- tile_values: float32 [8, 32, 128, 128, 128], P('row', 'col')
- tile_coords: int32 [8, 32, 128, 2], P('row', 'col'), may hold values from 0 to 271, as said below
- tile_count: int32 [8, 32], P('row', 'col'), may hold values from 16 to 128, as said below
- objective: float32 [262144], P('col')
- lower: float32 [262144], P('col'), may hold values from -2 to -0.2
- upper: float32 [262144], P('col'), may hold values from 0.2 to 2
- rhs: float32 [278528], P('row')
- primal_start: float32 [262144], P('col'), may hold values from -4 to 4
- dual_start: float32 [278528], P('row'), may hold values from 0 to 1
- step_size: float32 [1], replicated, may hold values from 0.02 to 0.06
Outputs:
- primal_solution: float32 [262144], P('col')
- dual_solution: float32 [278528], P('row')
The draws below stay inside these ranges and needn't reach their ends.
Inputs may be any that keep to these rules, and one draw needn't show every extreme that they name: `tile_coords`: coordinates are local: block rows 0 to 271, block columns 0 to 63, also in unused slots. Devices whose col index is congruent to their row index modulo the size of row hold one period: their block rows are (col index // size of row) * 64 plus 0 to 63. All other devices hold only linking block rows, 256 to 271. Every block row and every block column of A is met by some used slot. `tile_count`: period devices use all slots; other devices use 16 to 64 slots.
All inputs are finite; a program needn't handle non-finite values.
Results may differ from the reference program's by a relative error of at most 0.00012.
Values sent between devices are 32-bit elements; how exact they have to be, the bound alone decides.
No kernel may reach another device: no remote copies, remote signals or barrier semaphores. Data moves between devices by JAX's collectives and lax.ppermute only.
A program may use at most 64 MiB of HBM per device.

```python
import math
import jax
import jax.numpy as jnp
from jax import lax

TILE = 128
CB_DEV = 64
LINK_DEV = 16
RUIZ = 2
ITERS = 2
TILES_DEV = 128
RB_DEV = 272
ROWS = 278528
COLS = 262144
N_ROW = 8
N_COL = 32


def distinct_order(key, grid, length):
    scores = jax.random.randint(key, grid + (length,), 0, 1 << 20) * length + jnp.arange(length, dtype=jnp.int32)
    return jnp.argsort(scores, axis=-1).astype(jnp.int32)


def tile_layout(key):
    base = jax.random.fold_in(key, 7)
    keys = jax.random.split(base, 8)
    grid = (N_ROW, N_COL)
    row_ids = jnp.arange(N_ROW, dtype=jnp.int32)[:, None]
    col_ids = jnp.arange(N_COL, dtype=jnp.int32)[None, :]
    diagonal = col_ids % N_ROW == row_ids
    period_start = (col_ids // N_ROW * CB_DEV)[:, :, None]
    cover_cols = distinct_order(keys[0], grid, CB_DEV)
    extra_rows = jax.random.randint(keys[1], grid + (TILES_DEV - CB_DEV,), 0, CB_DEV)
    extra_cols = jax.random.randint(keys[2], grid + (TILES_DEV - CB_DEV,), 0, CB_DEV)
    cover_rows = jnp.broadcast_to(jnp.arange(CB_DEV, dtype=jnp.int32), grid + (CB_DEV,))
    period_rows = jnp.concatenate([cover_rows, extra_rows], axis=-1) + period_start
    period_cols = jnp.concatenate([cover_cols, extra_cols], axis=-1)
    shuffle = distinct_order(keys[3], grid, TILES_DEV)
    period_rows = jnp.take_along_axis(period_rows, shuffle, axis=-1)
    period_cols = jnp.take_along_axis(period_cols, shuffle, axis=-1)
    link_start = CB_DEV * (N_COL // N_ROW)
    link_cover = distinct_order(keys[4], grid, LINK_DEV)
    link_extra = jax.random.randint(keys[5], grid + (TILES_DEV - LINK_DEV,), 0, LINK_DEV)
    link_rows = jnp.concatenate([link_cover, link_extra], axis=-1) + link_start
    link_cols = jax.random.randint(keys[6], grid + (TILES_DEV,), 0, CB_DEV)
    block_rows = jnp.where(diagonal[:, :, None], period_rows, link_rows).astype(jnp.int32)
    block_cols = jnp.where(diagonal[:, :, None], period_cols, link_cols).astype(jnp.int32)
    drawn = jax.random.randint(keys[7], grid, LINK_DEV, CB_DEV + 1)
    pinned = (row_ids == 0) & (col_ids == 1)
    drawn = jnp.where(pinned, LINK_DEV, drawn)
    counts = jnp.where(diagonal, TILES_DEV, drawn).astype(jnp.int32)
    return (block_rows, block_cols, counts)


def draw_tile_coords(key, part):
    block_rows, block_cols, counts = tile_layout(key)
    return jnp.stack([block_rows, block_cols], axis=-1)


def draw_tile_count(key, part):
    block_rows, block_cols, counts = tile_layout(key)
    return counts


def draw_tile_values(key, part):
    block_rows, block_cols, counts = tile_layout(key)
    global_rows = jnp.arange(N_ROW, dtype=jnp.int32)[:, None, None] * RB_DEV + block_rows
    global_cols = jnp.arange(N_COL, dtype=jnp.int32)[None, :, None] * CB_DEV + block_cols
    keys = jax.random.split(jax.random.fold_in(key, 19), 3)
    shape = (N_ROW, N_COL, TILES_DEV, TILE, TILE)
    row_table = jnp.exp(jax.random.uniform(keys[0], (N_ROW * RB_DEV, TILE), jnp.float32, math.log(0.3), math.log(3.0)))
    col_table = jnp.exp(jax.random.uniform(keys[1], (N_COL * CB_DEV, TILE), jnp.float32, math.log(0.3), math.log(3.0)))
    entries = jax.random.normal(keys[2], shape, jnp.float32)
    return entries * row_table[global_rows][..., :, None] * col_table[global_cols][..., None, :]


def rising_vector(key, length):
    keys = jax.random.split(key, 2)
    position = jnp.arange(length, dtype=jnp.float32) / length
    spread = jnp.exp(jax.random.uniform(keys[0], (length,), jnp.float32, 0.0, math.log(10.0)))
    values = jax.random.normal(keys[1], (length,), jnp.float32)
    return 0.3 * values * spread * jnp.exp(position * math.log(3.0))


def draw_objective(key, part):
    return rising_vector(jax.random.fold_in(key, 31), COLS)


def draw_rhs(key, part):
    return rising_vector(jax.random.fold_in(key, 43), ROWS)


def block_levels(rng, dims, cuts, smallest, top_value):
    loudness = 1.0
    for dim, shards_of in cuts:
        heights = jax.random.uniform(jax.random.fold_in(jax.random.fold_in(rng, 6), dim), (shards_of,), jnp.float32, smallest / len(cuts), top_value / len(cuts))
        loudness = loudness * jnp.repeat(jnp.exp(heights), dims[dim] // shards_of).reshape((-1,) + (1,) * (len(dims) - 1 - dim))
    return loudness


def scatter_about(own_key, shape, width, most, cuts=(), kind=jnp.bfloat16):
    level = block_levels(own_key, shape, cuts, -0.22, 0.18) if cuts else 1.0
    values = jax.random.normal(own_key, shape, jnp.float32) * width * level
    return jnp.minimum(jnp.maximum(values, -most), most).astype(kind)


def setup_inputs(seed: int = 0) -> dict:
    seeds = jax.random.split(jax.random.key(seed), 11)
    return {
        "tile_values": draw_tile_values(jax.random.fold_in(seeds[10], 71), 0),
        "tile_coords": draw_tile_coords(jax.random.fold_in(seeds[10], 71), 0),
        "tile_count": draw_tile_count(jax.random.fold_in(seeds[10], 71), 0),
        "objective": draw_objective(jax.random.fold_in(seeds[10], 71), 0),
        "lower": jnp.clip(-2.0 + 1.8 * jax.random.uniform(seeds[4], (COLS,), jnp.float32) ** block_levels(seeds[4], (COLS,), ((0, 32),), -0.2, 0.2), -2.0, -0.2),
        "upper": jnp.clip(0.2 + 1.8 * jax.random.uniform(seeds[5], (COLS,), jnp.float32) ** block_levels(seeds[5], (COLS,), ((0, 32),), -0.2, 0.2), 0.2, 2.0),
        "rhs": draw_rhs(jax.random.fold_in(seeds[10], 71), 0),
        "primal_start": scatter_about(seeds[7], (COLS,), 1.0, 4.0, ((0, 32),), jnp.float32),
        "dual_start": jnp.clip(1.0 * jax.random.uniform(seeds[8], (ROWS,), jnp.float32) ** block_levels(seeds[8], (ROWS,), ((0, 8),), -0.2, 0.2), 0.0, 1.0),
        "step_size": jnp.clip(jax.random.uniform(seeds[9], (1,), jnp.float32, 0.02, 0.06), 0.02, 0.06),
    }


EPSILON = 1e-06
HIGHEST = lax.Precision.HIGHEST

def reference(tile_values, tile_coords, tile_count, objective, lower, upper, rhs, primal_start, dual_start, step_size):
    group_tiles = N_COL * TILES_DEV
    row_total = N_ROW * RB_DEV
    col_total = N_COL * CB_DEV
    slots = jnp.arange(TILES_DEV, dtype=jnp.int32)
    in_use = (slots[None, None, :] < tile_count[:, :, None]).astype(jnp.float32)
    global_rows = (jnp.arange(N_ROW, dtype=jnp.int32)[:, None, None] * RB_DEV + tile_coords[..., 0]).astype(jnp.int32)
    global_cols = (jnp.arange(N_COL, dtype=jnp.int32)[None, :, None] * CB_DEV + tile_coords[..., 1]).astype(jnp.int32)
    groups = (tile_values.reshape(N_ROW, group_tiles, TILE, TILE), global_rows.reshape(N_ROW, group_tiles), global_cols.reshape(N_ROW, group_tiles), in_use.reshape(N_ROW, group_tiles))
    flat_rows = global_rows.reshape(-1)
    flat_cols = global_cols.reshape(-1)
    row_scale = jnp.ones((row_total, TILE), jnp.float32)
    col_scale = jnp.ones((col_total, TILE), jnp.float32)
    for sweep in range(RUIZ):

        def peaks(group, row_scale=row_scale, col_scale=col_scale):
            values, row_index, col_index, used = group
            magnitude = jnp.abs(values) * used[:, None, None]
            row_local = lax.optimization_barrier(jnp.max(magnitude * col_scale[col_index][:, None, :], axis=2))
            col_local = lax.optimization_barrier(jnp.max(magnitude * row_scale[row_index][:, :, None], axis=1))
            return (row_local, col_local)
        row_local, col_local = lax.map(peaks, groups)
        row_peak = jnp.zeros((row_total, TILE), jnp.float32).at[flat_rows].max(row_local.reshape(-1, TILE))
        col_peak = jnp.zeros((col_total, TILE), jnp.float32).at[flat_cols].max(col_local.reshape(-1, TILE))
        row_scale = row_scale / jnp.sqrt(row_scale * row_peak + EPSILON)
        col_scale = col_scale / jnp.sqrt(col_scale * col_peak + EPSILON)

    def forward(vector):

        def partial_value(group):
            values, row_index, col_index, used = group
            products = jnp.einsum('tij,tj->ti', values, vector[col_index], precision=HIGHEST) * used[:, None]
            return jax.ops.segment_sum(products, row_index, num_segments=row_total)
        return lax.optimization_barrier(jnp.sum(lax.map(partial_value, groups), axis=0))

    def adjoint(vector):

        def partial_value(group):
            values, row_index, col_index, used = group
            products = jnp.einsum('tij,ti->tj', values, vector[row_index], precision=HIGHEST) * used[:, None]
            return jax.ops.segment_sum(products, col_index, num_segments=col_total)
        return lax.optimization_barrier(jnp.sum(lax.map(partial_value, groups), axis=0))
    cost = col_scale * objective.reshape(col_total, TILE)
    bound = row_scale * rhs.reshape(row_total, TILE)
    low_scaled = lower.reshape(col_total, TILE) / col_scale
    high_scaled = upper.reshape(col_total, TILE) / col_scale
    primal = primal_start.reshape(col_total, TILE) / col_scale
    dual = dual_start.reshape(row_total, TILE) / row_scale
    weight = jnp.sqrt(jnp.sum(cost * cost) + EPSILON) / jnp.sqrt(jnp.sum(bound * bound) + EPSILON)
    primal_step = step_size[0] / weight
    dual_step = step_size[0] * weight
    for iteration in range(ITERS):
        image = adjoint(row_scale * dual)
        moved = jnp.clip(primal - primal_step * (cost - col_scale * image), low_scaled, high_scaled)
        extra = 2.0 * moved - primal
        total = forward(col_scale * extra)
        dual = jnp.maximum(dual + dual_step * (bound - row_scale * total), 0.0)
        primal = moved
    return ((col_scale * primal).reshape(-1), (row_scale * dual).reshape(-1))
```

```python
import jax
import jax.numpy as jnp
from jax import lax
from jax.sharding import PartitionSpec as P

RUIZ = 2
ITERS = 2


EPSILON = 1e-06
HIGHEST = lax.Precision.HIGHEST


def butterfly(value, axis, size, combine):
    bit = 1
    while bit < size:
        pairs = [(i, i ^ bit) for i in range(size)]
        value = combine(value, lax.ppermute(value, axis, pairs))
        bit *= 2
    return value


def _max(a, b):
    return jax.tree.map(jnp.maximum, a, b)


def _add(a, b):
    return jax.tree.map(jnp.add, a, b)


def _max_add(a, b):
    return (jnp.maximum(a[0], b[0]), a[1] + b[1])


def make_local(n_row, n_col):
    def local(
        tile_values,
        tile_coords,
        tile_count,
        objective,
        lower,
        upper,
        rhs,
        primal_start,
        dual_start,
        step_size,
    ):
        tile_width = tile_values.shape[-1]
        slot_count = tile_values.shape[2]
        matrix = tile_values.reshape(slot_count, tile_width, tile_width)
        coords = tile_coords.reshape(slot_count, 2)
        block_rows = coords[:, 0]
        block_cols = coords[:, 1]
        row_blocks = rhs.shape[0] // tile_width
        col_blocks = objective.shape[0] // tile_width
        link_start = col_blocks * (n_col // n_row)
        r = lax.axis_index("row")
        c = lax.axis_index("col")
        is_period = (c % n_row) == r
        seg_start = (c // n_row) * col_blocks
        row_ids = jnp.arange(row_blocks, dtype=jnp.int32)[:, None]
        own_period = is_period & (row_ids >= seg_start) & (row_ids < seg_start + col_blocks)

        in_use = (jnp.arange(slot_count, dtype=jnp.int32) < tile_count.reshape(())).astype(jnp.float32)
        row_onehot = (jnp.arange(row_blocks, dtype=jnp.int32)[:, None] == block_rows[None, :]).astype(
            jnp.float32
        ) * in_use[None, :]
        col_onehot = (jnp.arange(col_blocks, dtype=jnp.int32)[:, None] == block_cols[None, :]).astype(
            jnp.float32
        ) * in_use[None, :]
        magnitude = jnp.abs(matrix) * in_use[:, None, None]

        def local_peaks(row_scale, col_scale):
            col_pieces = jnp.take(col_scale, block_cols, axis=0)
            row_pieces = jnp.take(row_scale, block_rows, axis=0)
            row_local = jnp.max(magnitude * col_pieces[:, None, :], axis=2)
            col_local = jnp.max(magnitude * row_pieces[:, :, None], axis=1)
            row_peak = jnp.zeros((row_blocks, tile_width), jnp.float32).at[block_rows].max(row_local)
            col_peak = jnp.zeros((col_blocks, tile_width), jnp.float32).at[block_cols].max(col_local)
            return row_peak, col_peak

        def rescale(scale, peak):
            return scale / jnp.sqrt(scale * peak + EPSILON)

        rhs_b = rhs.reshape(row_blocks, tile_width)
        obj_b = objective.reshape(col_blocks, tile_width)

        row_scale0 = jnp.ones((row_blocks, tile_width), jnp.float32)
        col_scale0 = jnp.ones((col_blocks, tile_width), jnp.float32)
        row_local1, col_local1 = local_peaks(row_scale0, col_scale0)
        link_peak1 = butterfly(row_local1[link_start:], "col", n_col, _max)
        col_peak1 = butterfly(col_local1, "row", n_row, _max)
        row_scale1 = rescale(row_scale0, jnp.concatenate([row_local1[:link_start], link_peak1], axis=0))
        col_scale1 = rescale(col_scale0, col_peak1)

        row_local2, col_local2 = local_peaks(row_scale1, col_scale1)
        own_scale2 = rescale(row_scale1, row_local2)
        own_bound = own_scale2 * rhs_b
        period_square = jnp.sum(jnp.where(own_period, own_bound * own_bound, 0.0)).reshape(1)
        link_peak2, period_total = butterfly((row_local2[link_start:], period_square), "col", n_col, _max_add)
        col_peak2 = butterfly(col_local2, "row", n_row, _max)
        row_scale = rescale(row_scale1, jnp.concatenate([row_local2[:link_start], link_peak2], axis=0))
        col_scale = rescale(col_scale1, col_peak2)

        cost = col_scale * obj_b
        bound = row_scale * rhs_b
        low_scaled = lower.reshape(col_blocks, tile_width) / col_scale
        high_scaled = upper.reshape(col_blocks, tile_width) / col_scale
        primal = primal_start.reshape(col_blocks, tile_width) / col_scale
        dual = dual_start.reshape(row_blocks, tile_width) / row_scale
        link_bound = bound[link_start:]
        bound_part = period_total + jnp.sum(link_bound * link_bound).reshape(1)
        cost_part = jnp.sum(cost * cost).reshape(1)

        def adjoint_local(dual):
            pieces = jnp.take(row_scale * dual, block_rows, axis=0)
            products = jnp.einsum("tij,ti->tj", matrix, pieces, precision=HIGHEST)
            return jnp.dot(col_onehot, products, precision=HIGHEST)

        def forward_local(extra):
            forward_pieces = jnp.take(col_scale * extra, block_cols, axis=0)
            forward_products = jnp.einsum("tij,tj->ti", matrix, forward_pieces, precision=HIGHEST)
            return jnp.dot(row_onehot, forward_products, precision=HIGHEST)

        image0_part = adjoint_local(dual)
        cost_total = butterfly(cost_part, "col", n_col, _add)
        image, bound_total = butterfly((image0_part, bound_part), "row", n_row, _add)
        weight = jnp.sqrt(cost_total[0] + EPSILON) / jnp.sqrt(bound_total[0] + EPSILON)
        primal_step = step_size[0] / weight
        dual_step = step_size[0] * weight

        for iteration in range(ITERS):
            if iteration > 0:
                image = butterfly(adjoint_local(dual), "row", n_row, _add)
            moved = jnp.clip(primal - primal_step * (cost - col_scale * image), low_scaled, high_scaled)
            extra = 2.0 * moved - primal
            partial_rows = forward_local(extra)
            primal = moved
            if iteration < ITERS - 1:
                link_total = butterfly(partial_rows[link_start:], "col", n_col, _add)
                total = jnp.concatenate([partial_rows[:link_start], link_total], axis=0)
                dual = jnp.maximum(dual + dual_step * (bound - row_scale * total), 0.0)
            else:
                own_dual = jnp.maximum(dual + dual_step * (bound - row_scale * partial_rows), 0.0)
                own_out = jnp.where(own_period, row_scale * own_dual, 0.0)
                joined = butterfly(
                    jnp.concatenate([own_out[:link_start], partial_rows[link_start:]], axis=0),
                    "col",
                    n_col,
                    _add,
                )
                link_dual = jnp.maximum(
                    dual[link_start:]
                    + dual_step * (bound[link_start:] - row_scale[link_start:] * joined[link_start:]),
                    0.0,
                )
                dual_out = jnp.concatenate([joined[:link_start], row_scale[link_start:] * link_dual], axis=0)
        return ((col_scale * primal).reshape(-1), dual_out.reshape(-1))

    return local


def solution(mesh):
    placed = (
        P("row", "col", None, None, None),
        P("row", "col", None, None),
        P("row", "col"),
        P("col"),
        P("col"),
        P("col"),
        P("row"),
        P("col"),
        P("row"),
        P(),
    )
    local = make_local(mesh.shape["row"], mesh.shape["col"])
    return jax.shard_map(
        local, mesh=mesh, in_specs=placed, out_specs=(P("col"), P("row")), check_vma=False
    )
```

```python
import jax
import jax.numpy as jnp
from jax import lax
from jax.sharding import PartitionSpec as P

RUIZ = 2
ITERS = 2


EPSILON = 1e-06
HIGHEST = lax.Precision.HIGHEST


def butterfly(value, axis, size, combine):
    bit = 1
    while bit < size:
        pairs = [(i, i ^ bit) for i in range(size)]
        value = combine(value, lax.ppermute(value, axis, pairs))
        bit *= 2
    return value


def _max(a, b):
    return jax.tree.map(jnp.maximum, a, b)


def _add(a, b):
    return jax.tree.map(jnp.add, a, b)


def make_local(n_row, n_col):
    def local(
        tile_values,
        tile_coords,
        tile_count,
        objective,
        lower,
        upper,
        rhs,
        primal_start,
        dual_start,
        step_size,
    ):
        tile_width = tile_values.shape[-1]
        slot_count = tile_values.shape[2]
        matrix = tile_values.reshape(slot_count, tile_width, tile_width)
        coords = tile_coords.reshape(slot_count, 2)
        block_rows = coords[:, 0]
        block_cols = coords[:, 1]
        row_blocks = rhs.shape[0] // tile_width
        col_blocks = objective.shape[0] // tile_width
        link_start = col_blocks * (n_col // n_row)
        r = lax.axis_index("row")
        c = lax.axis_index("col")
        is_period = (c % n_row) == r
        seg_start = (c // n_row) * col_blocks
        row_ids = jnp.arange(row_blocks, dtype=jnp.int32)[:, None]
        own_period = is_period & (row_ids >= seg_start) & (row_ids < seg_start + col_blocks)

        in_use = (jnp.arange(slot_count, dtype=jnp.int32) < tile_count.reshape(())).astype(jnp.float32)
        row_onehot = (jnp.arange(row_blocks, dtype=jnp.int32)[:, None] == block_rows[None, :]).astype(
            jnp.float32
        ) * in_use[None, :]
        col_onehot = (jnp.arange(col_blocks, dtype=jnp.int32)[:, None] == block_cols[None, :]).astype(
            jnp.float32
        ) * in_use[None, :]
        magnitude = jnp.abs(matrix) * in_use[:, None, None]

        def local_peaks(row_scale, col_scale):
            col_pieces = jnp.take(col_scale, block_cols, axis=0)
            row_pieces = jnp.take(row_scale, block_rows, axis=0)
            row_local = jnp.max(magnitude * col_pieces[:, None, :], axis=2)
            col_local = jnp.max(magnitude * row_pieces[:, :, None], axis=1)
            row_peak = jnp.zeros((row_blocks, tile_width), jnp.float32).at[block_rows].max(row_local)
            col_peak = jnp.zeros((col_blocks, tile_width), jnp.float32).at[block_cols].max(col_local)
            return row_peak, col_peak

        def rescale(scale, peak):
            return scale / jnp.sqrt(scale * peak + EPSILON)

        rhs_b = rhs.reshape(row_blocks, tile_width)
        obj_b = objective.reshape(col_blocks, tile_width)

        row_scale0 = jnp.ones((row_blocks, tile_width), jnp.float32)
        col_scale0 = jnp.ones((col_blocks, tile_width), jnp.float32)
        row_local1, col_local1 = local_peaks(row_scale0, col_scale0)
        link_peak1 = butterfly(row_local1[link_start:], "col", n_col, _max)
        col_peak1 = butterfly(col_local1, "row", n_row, _max)
        row_scale1 = rescale(row_scale0, jnp.concatenate([row_local1[:link_start], link_peak1], axis=0))
        col_scale1 = rescale(col_scale0, col_peak1)

        row_local2, col_local2 = local_peaks(row_scale1, col_scale1)
        own_scale2 = rescale(row_scale1, row_local2)
        own_bound = own_scale2 * rhs_b
        period_square = jnp.sum(jnp.where(own_period, own_bound * own_bound, 0.0))
        lanes = jnp.arange(tile_width, dtype=jnp.int32)[None, :]
        slot = jnp.where(is_period & (lanes == c // n_row), period_square, 0.0)
        packed2 = butterfly(jnp.concatenate([row_local2[link_start:], slot], axis=0), "col", n_col, _max)
        link_peak2 = packed2[: row_blocks - link_start]
        period_total = jnp.sum(packed2[row_blocks - link_start, : n_col // n_row]).reshape(1)
        col_peak2 = butterfly(col_local2, "row", n_row, _max)
        row_scale = rescale(row_scale1, jnp.concatenate([row_local2[:link_start], link_peak2], axis=0))
        col_scale = rescale(col_scale1, col_peak2)

        cost = col_scale * obj_b
        bound = row_scale * rhs_b
        low_scaled = lower.reshape(col_blocks, tile_width) / col_scale
        high_scaled = upper.reshape(col_blocks, tile_width) / col_scale
        primal = primal_start.reshape(col_blocks, tile_width) / col_scale
        dual = dual_start.reshape(row_blocks, tile_width) / row_scale
        link_bound = bound[link_start:]
        bound_part = period_total + jnp.sum(link_bound * link_bound).reshape(1)
        cost_part = jnp.sum(cost * cost).reshape(1)

        def adjoint_local(dual):
            pieces = jnp.take(row_scale * dual, block_rows, axis=0)
            products = jnp.einsum("tij,ti->tj", matrix, pieces, precision=HIGHEST)
            return jnp.dot(col_onehot, products, precision=HIGHEST)

        def forward_local(extra):
            forward_pieces = jnp.take(col_scale * extra, block_cols, axis=0)
            forward_products = jnp.einsum("tij,tj->ti", matrix, forward_pieces, precision=HIGHEST)
            return jnp.dot(row_onehot, forward_products, precision=HIGHEST)

        image0_part = adjoint_local(dual)
        cost_total = butterfly(cost_part, "col", n_col, _add)
        bound_row = jnp.where(lanes == 0, bound_part[0], 0.0)
        packed3 = butterfly(jnp.concatenate([image0_part, bound_row], axis=0), "row", n_row, _add)
        image = packed3[:col_blocks]
        bound_total = packed3[col_blocks, :1]
        weight = jnp.sqrt(cost_total[0] + EPSILON) / jnp.sqrt(bound_total[0] + EPSILON)
        primal_step = step_size[0] / weight
        dual_step = step_size[0] * weight

        for iteration in range(ITERS):
            if iteration > 0:
                image = butterfly(adjoint_local(dual), "row", n_row, _add)
            moved = jnp.clip(primal - primal_step * (cost - col_scale * image), low_scaled, high_scaled)
            extra = 2.0 * moved - primal
            partial_rows = forward_local(extra)
            primal = moved
            if iteration < ITERS - 1:
                link_total = butterfly(partial_rows[link_start:], "col", n_col, _add)
                total = jnp.concatenate([partial_rows[:link_start], link_total], axis=0)
                dual = jnp.maximum(dual + dual_step * (bound - row_scale * total), 0.0)
            else:
                own_dual = jnp.maximum(dual + dual_step * (bound - row_scale * partial_rows), 0.0)
                own_out = jnp.where(own_period, row_scale * own_dual, 0.0)
                joined = butterfly(
                    jnp.concatenate([own_out[:link_start], partial_rows[link_start:]], axis=0),
                    "col",
                    n_col,
                    _add,
                )
                link_dual = jnp.maximum(
                    dual[link_start:]
                    + dual_step * (bound[link_start:] - row_scale[link_start:] * joined[link_start:]),
                    0.0,
                )
                dual_out = jnp.concatenate([joined[:link_start], row_scale[link_start:] * link_dual], axis=0)
        return ((col_scale * primal).reshape(-1), dual_out.reshape(-1))

    return local


def solution(mesh):
    placed = (
        P("row", "col", None, None, None),
        P("row", "col", None, None),
        P("row", "col"),
        P("col"),
        P("col"),
        P("col"),
        P("row"),
        P("col"),
        P("row"),
        P(),
    )
    local = make_local(mesh.shape["row"], mesh.shape["col"])
    return jax.shard_map(
        local, mesh=mesh, in_specs=placed, out_specs=(P("col"), P("row")), check_vma=False
    )
```

```python
import jax
import jax.numpy as jnp
from jax import lax
from jax.sharding import PartitionSpec as P

RUIZ = 2
ITERS = 2


EPSILON = 1e-06
HIGHEST = lax.Precision.HIGHEST
HIGH = lax.Precision.HIGH


def butterfly(value, axis, size, combine):
    bit = 1
    while bit < size:
        pairs = [(i, i ^ bit) for i in range(size)]
        value = combine(value, lax.ppermute(value, axis, pairs))
        bit *= 2
    return value


def _max(a, b):
    return jax.tree.map(jnp.maximum, a, b)


def _add(a, b):
    return jax.tree.map(jnp.add, a, b)


def make_local(n_row, n_col):
    def local(
        tile_values,
        tile_coords,
        tile_count,
        objective,
        lower,
        upper,
        rhs,
        primal_start,
        dual_start,
        step_size,
    ):
        tile_width = tile_values.shape[-1]
        slot_count = tile_values.shape[2]
        matrix = tile_values.reshape(slot_count, tile_width, tile_width)
        coords = tile_coords.reshape(slot_count, 2)
        block_rows = coords[:, 0]
        block_cols = coords[:, 1]
        row_blocks = rhs.shape[0] // tile_width
        col_blocks = objective.shape[0] // tile_width
        link_start = col_blocks * (n_col // n_row)
        r = lax.axis_index("row")
        c = lax.axis_index("col")
        is_period = (c % n_row) == r
        seg_start = (c // n_row) * col_blocks
        row_ids = jnp.arange(row_blocks, dtype=jnp.int32)[:, None]
        own_period = is_period & (row_ids >= seg_start) & (row_ids < seg_start + col_blocks)

        in_use = (jnp.arange(slot_count, dtype=jnp.int32) < tile_count.reshape(())).astype(jnp.float32)
        row_onehot = (jnp.arange(row_blocks, dtype=jnp.int32)[:, None] == block_rows[None, :]).astype(
            jnp.float32
        ) * in_use[None, :]
        col_onehot = (jnp.arange(col_blocks, dtype=jnp.int32)[:, None] == block_cols[None, :]).astype(
            jnp.float32
        ) * in_use[None, :]
        magnitude = jnp.abs(matrix) * in_use[:, None, None]

        def local_peaks(row_scale, col_scale):
            col_pieces = jnp.take(col_scale, block_cols, axis=0)
            row_pieces = jnp.take(row_scale, block_rows, axis=0)
            row_local = jnp.max(magnitude * col_pieces[:, None, :], axis=2)
            col_local = jnp.max(magnitude * row_pieces[:, :, None], axis=1)
            row_peak = jnp.zeros((row_blocks, tile_width), jnp.float32).at[block_rows].max(row_local)
            col_peak = jnp.zeros((col_blocks, tile_width), jnp.float32).at[block_cols].max(col_local)
            return row_peak, col_peak

        def rescale(scale, peak):
            return scale / jnp.sqrt(scale * peak + EPSILON)

        rhs_b = rhs.reshape(row_blocks, tile_width)
        obj_b = objective.reshape(col_blocks, tile_width)

        row_scale0 = jnp.ones((row_blocks, tile_width), jnp.float32)
        col_scale0 = jnp.ones((col_blocks, tile_width), jnp.float32)
        row_local1, col_local1 = local_peaks(row_scale0, col_scale0)
        link_peak1 = butterfly(row_local1[link_start:], "col", n_col, _max)
        col_peak1 = butterfly(col_local1, "row", n_row, _max)
        row_scale1 = rescale(row_scale0, jnp.concatenate([row_local1[:link_start], link_peak1], axis=0))
        col_scale1 = rescale(col_scale0, col_peak1)

        row_local2, col_local2 = local_peaks(row_scale1, col_scale1)
        own_scale2 = rescale(row_scale1, row_local2)
        own_bound = own_scale2 * rhs_b
        period_square = jnp.sum(jnp.where(own_period, own_bound * own_bound, 0.0))
        lanes = jnp.arange(tile_width, dtype=jnp.int32)[None, :]
        slot = jnp.where(is_period & (lanes == c // n_row), period_square, 0.0)
        packed2 = butterfly(jnp.concatenate([row_local2[link_start:], slot], axis=0), "col", n_col, _max)
        link_peak2 = packed2[: row_blocks - link_start]
        period_total = jnp.sum(packed2[row_blocks - link_start, : n_col // n_row]).reshape(1)
        col_peak2 = butterfly(col_local2, "row", n_row, _max)
        row_scale = rescale(row_scale1, jnp.concatenate([row_local2[:link_start], link_peak2], axis=0))
        col_scale = rescale(col_scale1, col_peak2)

        cost = col_scale * obj_b
        bound = row_scale * rhs_b
        low_scaled = lower.reshape(col_blocks, tile_width) / col_scale
        high_scaled = upper.reshape(col_blocks, tile_width) / col_scale
        primal = primal_start.reshape(col_blocks, tile_width) / col_scale
        dual = dual_start.reshape(row_blocks, tile_width) / row_scale
        link_bound = bound[link_start:]
        bound_part = period_total + jnp.sum(link_bound * link_bound).reshape(1)
        cost_part = jnp.sum(cost * cost).reshape(1)

        def adjoint_local(dual):
            pieces = jnp.take(row_scale * dual, block_rows, axis=0)
            products = jnp.einsum("tij,ti->tj", matrix, pieces, precision=HIGH)
            return jnp.dot(col_onehot, products, precision=HIGHEST)

        def forward_local(extra):
            forward_pieces = jnp.take(col_scale * extra, block_cols, axis=0)
            forward_products = jnp.einsum("tij,tj->ti", matrix, forward_pieces, precision=HIGH)
            return jnp.dot(row_onehot, forward_products, precision=HIGHEST)

        image0_part = adjoint_local(dual)
        cost_total = butterfly(cost_part, "col", n_col, _add)
        bound_row = jnp.where(lanes == 0, bound_part[0], 0.0)
        packed3 = butterfly(jnp.concatenate([image0_part, bound_row], axis=0), "row", n_row, _add)
        image = packed3[:col_blocks]
        bound_total = packed3[col_blocks, :1]
        weight = jnp.sqrt(cost_total[0] + EPSILON) / jnp.sqrt(bound_total[0] + EPSILON)
        primal_step = step_size[0] / weight
        dual_step = step_size[0] * weight

        for iteration in range(ITERS):
            if iteration > 0:
                image = butterfly(adjoint_local(dual), "row", n_row, _add)
            moved = jnp.clip(primal - primal_step * (cost - col_scale * image), low_scaled, high_scaled)
            extra = 2.0 * moved - primal
            partial_rows = forward_local(extra)
            primal = moved
            if iteration < ITERS - 1:
                link_total = butterfly(partial_rows[link_start:], "col", n_col, _add)
                total = jnp.concatenate([partial_rows[:link_start], link_total], axis=0)
                dual = jnp.maximum(dual + dual_step * (bound - row_scale * total), 0.0)
            else:
                own_dual = jnp.maximum(dual + dual_step * (bound - row_scale * partial_rows), 0.0)
                own_out = jnp.where(own_period, row_scale * own_dual, 0.0)
                joined = butterfly(
                    jnp.concatenate([own_out[:link_start], partial_rows[link_start:]], axis=0),
                    "col",
                    n_col,
                    _add,
                )
                link_dual = jnp.maximum(
                    dual[link_start:]
                    + dual_step * (bound[link_start:] - row_scale[link_start:] * joined[link_start:]),
                    0.0,
                )
                dual_out = jnp.concatenate([joined[:link_start], row_scale[link_start:] * link_dual], axis=0)
        return ((col_scale * primal).reshape(-1), dual_out.reshape(-1))

    return local


def solution(mesh):
    placed = (
        P("row", "col", None, None, None),
        P("row", "col", None, None),
        P("row", "col"),
        P("col"),
        P("col"),
        P("col"),
        P("row"),
        P("col"),
        P("row"),
        P(),
    )
    local = make_local(mesh.shape["row"], mesh.shape["col"])
    return jax.shard_map(
        local, mesh=mesh, in_specs=placed, out_specs=(P("col"), P("row")), check_vma=False
    )
```

```python
import jax
import jax.numpy as jnp
from jax import lax
from jax.sharding import PartitionSpec as P

RUIZ = 2
ITERS = 2


EPSILON = 1e-06
HIGHEST = lax.Precision.HIGHEST
HIGH = lax.Precision.HIGH


def butterfly(value, axis, size, combine):
    bit = 1
    while bit < size:
        pairs = [(i, i ^ bit) for i in range(size)]
        value = combine(value, lax.ppermute(value, axis, pairs))
        bit *= 2
    return value


def _max(a, b):
    return jax.tree.map(jnp.maximum, a, b)


def _add(a, b):
    return jax.tree.map(jnp.add, a, b)


def make_local(n_row, n_col):
    def local(
        tile_values,
        tile_coords,
        tile_count,
        objective,
        lower,
        upper,
        rhs,
        primal_start,
        dual_start,
        step_size,
    ):
        tile_width = tile_values.shape[-1]
        slot_count = tile_values.shape[2]
        matrix = tile_values.reshape(slot_count, tile_width, tile_width)
        coords = tile_coords.reshape(slot_count, 2)
        block_rows = coords[:, 0]
        block_cols = coords[:, 1]
        row_blocks = rhs.shape[0] // tile_width
        col_blocks = objective.shape[0] // tile_width
        link_start = col_blocks * (n_col // n_row)
        r = lax.axis_index("row")
        c = lax.axis_index("col")
        is_period = (c % n_row) == r
        seg_start = (c // n_row) * col_blocks
        row_ids = jnp.arange(row_blocks, dtype=jnp.int32)[:, None]
        own_period = is_period & (row_ids >= seg_start) & (row_ids < seg_start + col_blocks)

        in_use = (jnp.arange(slot_count, dtype=jnp.int32) < tile_count.reshape(())).astype(jnp.float32)
        row_onehot = (jnp.arange(row_blocks, dtype=jnp.int32)[:, None] == block_rows[None, :]).astype(
            jnp.float32
        ) * in_use[None, :]
        col_onehot = (jnp.arange(col_blocks, dtype=jnp.int32)[:, None] == block_cols[None, :]).astype(
            jnp.float32
        ) * in_use[None, :]
        magnitude = jnp.abs(matrix) * in_use[:, None, None]

        def row_peaks(col_scale):
            col_pieces = jnp.take(col_scale, block_cols, axis=0)
            row_local = jnp.max(magnitude * col_pieces[:, None, :], axis=2)
            return jnp.zeros((row_blocks, tile_width), jnp.float32).at[block_rows].max(row_local)

        def col_peaks(row_scale):
            row_pieces = jnp.take(row_scale, block_rows, axis=0)
            col_local = jnp.max(magnitude * row_pieces[:, :, None], axis=1)
            return jnp.zeros((col_blocks, tile_width), jnp.float32).at[block_cols].max(col_local)

        def rescale(scale, peak):
            return scale / jnp.sqrt(scale * peak + EPSILON)

        rhs_b = rhs.reshape(row_blocks, tile_width)
        obj_b = objective.reshape(col_blocks, tile_width)
        lanes = jnp.arange(tile_width, dtype=jnp.int32)[None, :]

        row_scale0 = jnp.ones((row_blocks, tile_width), jnp.float32)
        col_scale0 = jnp.ones((col_blocks, tile_width), jnp.float32)
        row_local1 = row_peaks(col_scale0)
        link_peak1 = butterfly(row_local1[link_start:], "col", n_col, _max)
        row_scale1 = rescale(row_scale0, jnp.concatenate([row_local1[:link_start], link_peak1], axis=0))
        col_local1 = col_peaks(row_scale0)
        col_local2 = col_peaks(row_scale1)
        col_both = butterfly(jnp.concatenate([col_local1, col_local2], axis=0), "row", n_row, _max)
        col_scale1 = rescale(col_scale0, col_both[:col_blocks])
        col_scale = rescale(col_scale1, col_both[col_blocks:])

        row_local2 = row_peaks(col_scale1)
        own_scale2 = rescale(row_scale1, row_local2)
        own_bound = own_scale2 * rhs_b
        period_square = jnp.sum(jnp.where(own_period, own_bound * own_bound, 0.0))
        cost = col_scale * obj_b
        cost_square = jnp.sum(cost * cost)
        slot = jnp.where(lanes == c, cost_square, 0.0)
        slot = jnp.where(is_period & (lanes == n_col + c // n_row), period_square, slot)
        packed2 = butterfly(jnp.concatenate([row_local2[link_start:], slot], axis=0), "col", n_col, _max)
        link_peak2 = packed2[: row_blocks - link_start]
        spare = packed2[row_blocks - link_start]
        cost_total = jnp.sum(spare[:n_col]).reshape(1)
        period_total = jnp.sum(spare[n_col : n_col + n_col // n_row]).reshape(1)
        row_scale = rescale(row_scale1, jnp.concatenate([row_local2[:link_start], link_peak2], axis=0))

        bound = row_scale * rhs_b
        low_scaled = lower.reshape(col_blocks, tile_width) / col_scale
        high_scaled = upper.reshape(col_blocks, tile_width) / col_scale
        primal = primal_start.reshape(col_blocks, tile_width) / col_scale
        dual = dual_start.reshape(row_blocks, tile_width) / row_scale
        link_bound = bound[link_start:]
        bound_part = period_total + jnp.sum(link_bound * link_bound).reshape(1)

        def adjoint_local(dual):
            pieces = jnp.take(row_scale * dual, block_rows, axis=0)
            products = jnp.einsum("tij,ti->tj", matrix, pieces, precision=HIGH)
            return jnp.dot(col_onehot, products, precision=HIGHEST)

        def forward_local(extra):
            forward_pieces = jnp.take(col_scale * extra, block_cols, axis=0)
            forward_products = jnp.einsum("tij,tj->ti", matrix, forward_pieces, precision=HIGH)
            return jnp.dot(row_onehot, forward_products, precision=HIGHEST)

        image0_part = adjoint_local(dual)
        bound_row = jnp.where(lanes == 0, bound_part[0], 0.0)
        packed3 = butterfly(jnp.concatenate([image0_part, bound_row], axis=0), "row", n_row, _add)
        image = packed3[:col_blocks]
        bound_total = packed3[col_blocks, :1]
        weight = jnp.sqrt(cost_total[0] + EPSILON) / jnp.sqrt(bound_total[0] + EPSILON)
        primal_step = step_size[0] / weight
        dual_step = step_size[0] * weight

        for iteration in range(ITERS):
            if iteration > 0:
                image = butterfly(adjoint_local(dual), "row", n_row, _add)
            moved = jnp.clip(primal - primal_step * (cost - col_scale * image), low_scaled, high_scaled)
            extra = 2.0 * moved - primal
            partial_rows = forward_local(extra)
            primal = moved
            if iteration < ITERS - 1:
                link_total = butterfly(partial_rows[link_start:], "col", n_col, _add)
                total = jnp.concatenate([partial_rows[:link_start], link_total], axis=0)
                dual = jnp.maximum(dual + dual_step * (bound - row_scale * total), 0.0)
            else:
                own_dual = jnp.maximum(dual + dual_step * (bound - row_scale * partial_rows), 0.0)
                own_out = jnp.where(own_period, row_scale * own_dual, 0.0)
                joined = butterfly(
                    jnp.concatenate([own_out[:link_start], partial_rows[link_start:]], axis=0),
                    "col",
                    n_col,
                    _add,
                )
                link_dual = jnp.maximum(
                    dual[link_start:]
                    + dual_step * (bound[link_start:] - row_scale[link_start:] * joined[link_start:]),
                    0.0,
                )
                dual_out = jnp.concatenate([joined[:link_start], row_scale[link_start:] * link_dual], axis=0)
        return ((col_scale * primal).reshape(-1), dual_out.reshape(-1))

    return local


def solution(mesh):
    placed = (
        P("row", "col", None, None, None),
        P("row", "col", None, None),
        P("row", "col"),
        P("col"),
        P("col"),
        P("col"),
        P("row"),
        P("col"),
        P("row"),
        P(),
    )
    local = make_local(mesh.shape["row"], mesh.shape["col"])
    return jax.shard_map(
        local, mesh=mesh, in_specs=placed, out_specs=(P("col"), P("row")), check_vma=False
    )
```

```python
import jax
import jax.numpy as jnp
from jax import lax
from jax.sharding import PartitionSpec as P

RUIZ = 2
ITERS = 2


EPSILON = 1e-06
HIGHEST = lax.Precision.HIGHEST
HIGH = lax.Precision.HIGH


def butterfly(value, axis, size, combine):
    bit = 1
    while bit < size:
        pairs = [(i, i ^ bit) for i in range(size)]
        value = combine(value, lax.ppermute(value, axis, pairs))
        bit *= 2
    return value


def exchange(value, axis, size, reduce):
    spread = jnp.broadcast_to(value[None], (size,) + value.shape)
    return reduce(lax.all_to_all(spread, axis, 0, 0, tiled=False), axis=0)


def _max(a, b):
    return jax.tree.map(jnp.maximum, a, b)


def _add(a, b):
    return jax.tree.map(jnp.add, a, b)


def make_local(n_row, n_col):
    def local(
        tile_values,
        tile_coords,
        tile_count,
        objective,
        lower,
        upper,
        rhs,
        primal_start,
        dual_start,
        step_size,
    ):
        tile_width = tile_values.shape[-1]
        slot_count = tile_values.shape[2]
        matrix = tile_values.reshape(slot_count, tile_width, tile_width)
        coords = tile_coords.reshape(slot_count, 2)
        block_rows = coords[:, 0]
        block_cols = coords[:, 1]
        row_blocks = rhs.shape[0] // tile_width
        col_blocks = objective.shape[0] // tile_width
        link_start = col_blocks * (n_col // n_row)
        r = lax.axis_index("row")
        c = lax.axis_index("col")
        is_period = (c % n_row) == r
        seg_start = (c // n_row) * col_blocks
        row_ids = jnp.arange(row_blocks, dtype=jnp.int32)[:, None]
        own_period = is_period & (row_ids >= seg_start) & (row_ids < seg_start + col_blocks)

        in_use = (jnp.arange(slot_count, dtype=jnp.int32) < tile_count.reshape(())).astype(jnp.float32)
        row_onehot = (jnp.arange(row_blocks, dtype=jnp.int32)[:, None] == block_rows[None, :]).astype(
            jnp.float32
        ) * in_use[None, :]
        col_onehot = (jnp.arange(col_blocks, dtype=jnp.int32)[:, None] == block_cols[None, :]).astype(
            jnp.float32
        ) * in_use[None, :]
        magnitude = jnp.abs(matrix) * in_use[:, None, None]

        def row_peaks(col_scale):
            col_pieces = jnp.take(col_scale, block_cols, axis=0)
            row_local = jnp.max(magnitude * col_pieces[:, None, :], axis=2)
            return jnp.zeros((row_blocks, tile_width), jnp.float32).at[block_rows].max(row_local)

        def col_peaks(row_scale):
            row_pieces = jnp.take(row_scale, block_rows, axis=0)
            col_local = jnp.max(magnitude * row_pieces[:, :, None], axis=1)
            return jnp.zeros((col_blocks, tile_width), jnp.float32).at[block_cols].max(col_local)

        def rescale(scale, peak):
            return scale / jnp.sqrt(scale * peak + EPSILON)

        rhs_b = rhs.reshape(row_blocks, tile_width)
        obj_b = objective.reshape(col_blocks, tile_width)
        lanes = jnp.arange(tile_width, dtype=jnp.int32)[None, :]

        row_scale0 = jnp.ones((row_blocks, tile_width), jnp.float32)
        col_scale0 = jnp.ones((col_blocks, tile_width), jnp.float32)
        row_local1 = row_peaks(col_scale0)
        link_peak1 = exchange(row_local1[link_start:], "col", n_col, jnp.max)
        row_scale1 = rescale(row_scale0, jnp.concatenate([row_local1[:link_start], link_peak1], axis=0))
        col_local1 = col_peaks(row_scale0)
        col_local2 = col_peaks(row_scale1)
        col_both = exchange(jnp.concatenate([col_local1, col_local2], axis=0), "row", n_row, jnp.max)
        col_scale1 = rescale(col_scale0, col_both[:col_blocks])
        col_scale = rescale(col_scale1, col_both[col_blocks:])

        row_local2 = row_peaks(col_scale1)
        own_scale2 = rescale(row_scale1, row_local2)
        own_bound = own_scale2 * rhs_b
        period_square = jnp.sum(jnp.where(own_period, own_bound * own_bound, 0.0))
        cost = col_scale * obj_b
        cost_square = jnp.sum(cost * cost)
        slot = jnp.where(lanes == c, cost_square, 0.0)
        slot = jnp.where(is_period & (lanes == n_col + c // n_row), period_square, slot)
        packed2 = exchange(jnp.concatenate([row_local2[link_start:], slot], axis=0), "col", n_col, jnp.max)
        link_peak2 = packed2[: row_blocks - link_start]
        spare = packed2[row_blocks - link_start]
        cost_total = jnp.sum(spare[:n_col]).reshape(1)
        period_total = jnp.sum(spare[n_col : n_col + n_col // n_row]).reshape(1)
        row_scale = rescale(row_scale1, jnp.concatenate([row_local2[:link_start], link_peak2], axis=0))

        bound = row_scale * rhs_b
        low_scaled = lower.reshape(col_blocks, tile_width) / col_scale
        high_scaled = upper.reshape(col_blocks, tile_width) / col_scale
        primal = primal_start.reshape(col_blocks, tile_width) / col_scale
        dual = dual_start.reshape(row_blocks, tile_width) / row_scale
        link_bound = bound[link_start:]
        bound_part = period_total + jnp.sum(link_bound * link_bound).reshape(1)

        def adjoint_local(dual):
            pieces = jnp.take(row_scale * dual, block_rows, axis=0)
            products = jnp.einsum("tij,ti->tj", matrix, pieces, precision=HIGH)
            return jnp.dot(col_onehot, products, precision=HIGHEST)

        def forward_local(extra):
            forward_pieces = jnp.take(col_scale * extra, block_cols, axis=0)
            forward_products = jnp.einsum("tij,tj->ti", matrix, forward_pieces, precision=HIGH)
            return jnp.dot(row_onehot, forward_products, precision=HIGHEST)

        image0_part = adjoint_local(dual)
        bound_row = jnp.where(lanes == 0, bound_part[0], 0.0)
        packed3 = exchange(jnp.concatenate([image0_part, bound_row], axis=0), "row", n_row, jnp.sum)
        image = packed3[:col_blocks]
        bound_total = packed3[col_blocks, :1]
        weight = jnp.sqrt(cost_total[0] + EPSILON) / jnp.sqrt(bound_total[0] + EPSILON)
        primal_step = step_size[0] / weight
        dual_step = step_size[0] * weight

        for iteration in range(ITERS):
            if iteration > 0:
                image = exchange(adjoint_local(dual), "row", n_row, jnp.sum)
            moved = jnp.clip(primal - primal_step * (cost - col_scale * image), low_scaled, high_scaled)
            extra = 2.0 * moved - primal
            partial_rows = forward_local(extra)
            primal = moved
            if iteration < ITERS - 1:
                link_total = exchange(partial_rows[link_start:], "col", n_col, jnp.sum)
                total = jnp.concatenate([partial_rows[:link_start], link_total], axis=0)
                dual = jnp.maximum(dual + dual_step * (bound - row_scale * total), 0.0)
            else:
                own_dual = jnp.maximum(dual + dual_step * (bound - row_scale * partial_rows), 0.0)
                own_out = jnp.where(own_period, row_scale * own_dual, 0.0)
                joined = butterfly(
                    jnp.concatenate([own_out[:link_start], partial_rows[link_start:]], axis=0),
                    "col",
                    n_col,
                    _add,
                )
                link_dual = jnp.maximum(
                    dual[link_start:]
                    + dual_step * (bound[link_start:] - row_scale[link_start:] * joined[link_start:]),
                    0.0,
                )
                dual_out = jnp.concatenate([joined[:link_start], row_scale[link_start:] * link_dual], axis=0)
        return ((col_scale * primal).reshape(-1), dual_out.reshape(-1))

    return local


def solution(mesh):
    placed = (
        P("row", "col", None, None, None),
        P("row", "col", None, None),
        P("row", "col"),
        P("col"),
        P("col"),
        P("col"),
        P("row"),
        P("col"),
        P("row"),
        P(),
    )
    local = make_local(mesh.shape["row"], mesh.shape["col"])
    return jax.shard_map(
        local, mesh=mesh, in_specs=placed, out_specs=(P("col"), P("row")), check_vma=False
    )
```

```python
import jax
import jax.numpy as jnp
from jax import lax
from jax.sharding import PartitionSpec as P

RUIZ = 2
ITERS = 2


EPSILON = 1e-06
HIGHEST = lax.Precision.HIGHEST
HIGH = lax.Precision.HIGH


def butterfly(value, axis, size, combine):
    bit = 1
    while bit < size:
        pairs = [(i, i ^ bit) for i in range(size)]
        value = combine(value, lax.ppermute(value, axis, pairs))
        bit *= 2
    return value


def exchange(value, axis, size, reduce):
    spread = jnp.broadcast_to(value[None], (size,) + value.shape)
    return reduce(lax.all_to_all(spread, axis, 0, 0, tiled=False), axis=0)


def _max(a, b):
    return jax.tree.map(jnp.maximum, a, b)


def _add(a, b):
    return jax.tree.map(jnp.add, a, b)


def make_local(n_row, n_col):
    def local(
        tile_values,
        tile_coords,
        tile_count,
        objective,
        lower,
        upper,
        rhs,
        primal_start,
        dual_start,
        step_size,
    ):
        tile_width = tile_values.shape[-1]
        slot_count = tile_values.shape[2]
        matrix = tile_values.reshape(slot_count, tile_width, tile_width)
        coords = tile_coords.reshape(slot_count, 2)
        block_rows = coords[:, 0]
        block_cols = coords[:, 1]
        row_blocks = rhs.shape[0] // tile_width
        col_blocks = objective.shape[0] // tile_width
        link_start = col_blocks * (n_col // n_row)
        r = lax.axis_index("row")
        c = lax.axis_index("col")
        is_period = (c % n_row) == r
        seg_start = (c // n_row) * col_blocks
        row_ids = jnp.arange(row_blocks, dtype=jnp.int32)[:, None]
        own_period = is_period & (row_ids >= seg_start) & (row_ids < seg_start + col_blocks)

        in_use = (jnp.arange(slot_count, dtype=jnp.int32) < tile_count.reshape(())).astype(jnp.float32)
        row_onehot = (jnp.arange(row_blocks, dtype=jnp.int32)[:, None] == block_rows[None, :]).astype(
            jnp.float32
        ) * in_use[None, :]
        col_onehot = (jnp.arange(col_blocks, dtype=jnp.int32)[:, None] == block_cols[None, :]).astype(
            jnp.float32
        ) * in_use[None, :]
        magnitude = jnp.abs(matrix) * in_use[:, None, None]

        def row_peaks(col_scale):
            col_pieces = jnp.take(col_scale, block_cols, axis=0)
            row_local = jnp.max(magnitude * col_pieces[:, None, :], axis=2)
            return jnp.zeros((row_blocks, tile_width), jnp.float32).at[block_rows].max(row_local)

        def col_peaks(row_scale):
            row_pieces = jnp.take(row_scale, block_rows, axis=0)
            col_local = jnp.max(magnitude * row_pieces[:, :, None], axis=1)
            return jnp.zeros((col_blocks, tile_width), jnp.float32).at[block_cols].max(col_local)

        def rescale(scale, peak):
            return scale / jnp.sqrt(scale * peak + EPSILON)

        rhs_b = rhs.reshape(row_blocks, tile_width)
        obj_b = objective.reshape(col_blocks, tile_width)
        lanes = jnp.arange(tile_width, dtype=jnp.int32)[None, :]

        row_scale0 = jnp.ones((row_blocks, tile_width), jnp.float32)
        col_scale0 = jnp.ones((col_blocks, tile_width), jnp.float32)
        row_local1 = row_peaks(col_scale0)
        link_peak1 = exchange(row_local1[link_start:], "col", n_col, jnp.max)
        row_scale1 = rescale(row_scale0, jnp.concatenate([row_local1[:link_start], link_peak1], axis=0))
        col_local1 = col_peaks(row_scale0)
        col_local2 = col_peaks(row_scale1)
        col_both = butterfly(jnp.concatenate([col_local1, col_local2], axis=0), "row", n_row, _max)
        col_scale1 = rescale(col_scale0, col_both[:col_blocks])
        col_scale = rescale(col_scale1, col_both[col_blocks:])

        row_local2 = row_peaks(col_scale1)
        own_scale2 = rescale(row_scale1, row_local2)
        own_bound = own_scale2 * rhs_b
        period_square = jnp.sum(jnp.where(own_period, own_bound * own_bound, 0.0))
        cost = col_scale * obj_b
        cost_square = jnp.sum(cost * cost)
        slot = jnp.where(lanes == c, cost_square, 0.0)
        slot = jnp.where(is_period & (lanes == n_col + c // n_row), period_square, slot)
        packed2 = exchange(jnp.concatenate([row_local2[link_start:], slot], axis=0), "col", n_col, jnp.max)
        link_peak2 = packed2[: row_blocks - link_start]
        spare = packed2[row_blocks - link_start]
        cost_total = jnp.sum(spare[:n_col]).reshape(1)
        period_total = jnp.sum(spare[n_col : n_col + n_col // n_row]).reshape(1)
        row_scale = rescale(row_scale1, jnp.concatenate([row_local2[:link_start], link_peak2], axis=0))

        bound = row_scale * rhs_b
        low_scaled = lower.reshape(col_blocks, tile_width) / col_scale
        high_scaled = upper.reshape(col_blocks, tile_width) / col_scale
        primal = primal_start.reshape(col_blocks, tile_width) / col_scale
        dual = dual_start.reshape(row_blocks, tile_width) / row_scale
        link_bound = bound[link_start:]
        bound_part = period_total + jnp.sum(link_bound * link_bound).reshape(1)

        def adjoint_local(dual):
            pieces = jnp.take(row_scale * dual, block_rows, axis=0)
            products = jnp.einsum("tij,ti->tj", matrix, pieces, precision=HIGH)
            return jnp.dot(col_onehot, products, precision=HIGHEST)

        def forward_local(extra):
            forward_pieces = jnp.take(col_scale * extra, block_cols, axis=0)
            forward_products = jnp.einsum("tij,tj->ti", matrix, forward_pieces, precision=HIGH)
            return jnp.dot(row_onehot, forward_products, precision=HIGHEST)

        image0_part = adjoint_local(dual)
        bound_row = jnp.where(lanes == 0, bound_part[0], 0.0)
        packed3 = exchange(jnp.concatenate([image0_part, bound_row], axis=0), "row", n_row, jnp.sum)
        image = packed3[:col_blocks]
        bound_total = packed3[col_blocks, :1]
        weight = jnp.sqrt(cost_total[0] + EPSILON) / jnp.sqrt(bound_total[0] + EPSILON)
        primal_step = step_size[0] / weight
        dual_step = step_size[0] * weight

        for iteration in range(ITERS):
            if iteration > 0:
                image = exchange(adjoint_local(dual), "row", n_row, jnp.sum)
            moved = jnp.clip(primal - primal_step * (cost - col_scale * image), low_scaled, high_scaled)
            extra = 2.0 * moved - primal
            partial_rows = forward_local(extra)
            primal = moved
            if iteration < ITERS - 1:
                link_total = exchange(partial_rows[link_start:], "col", n_col, jnp.sum)
                total = jnp.concatenate([partial_rows[:link_start], link_total], axis=0)
                dual = jnp.maximum(dual + dual_step * (bound - row_scale * total), 0.0)
            else:
                own_dual = jnp.maximum(dual + dual_step * (bound - row_scale * partial_rows), 0.0)
                own_out = jnp.where(own_period, row_scale * own_dual, 0.0)
                joined = butterfly(
                    jnp.concatenate([own_out[:link_start], partial_rows[link_start:]], axis=0),
                    "col",
                    n_col,
                    _add,
                )
                link_dual = jnp.maximum(
                    dual[link_start:]
                    + dual_step * (bound[link_start:] - row_scale[link_start:] * joined[link_start:]),
                    0.0,
                )
                dual_out = jnp.concatenate([joined[:link_start], row_scale[link_start:] * link_dual], axis=0)
        return ((col_scale * primal).reshape(-1), dual_out.reshape(-1))

    return local


def solution(mesh):
    placed = (
        P("row", "col", None, None, None),
        P("row", "col", None, None),
        P("row", "col"),
        P("col"),
        P("col"),
        P("col"),
        P("row"),
        P("col"),
        P("row"),
        P(),
    )
    local = make_local(mesh.shape["row"], mesh.shape["col"])
    return jax.shard_map(
        local, mesh=mesh, in_specs=placed, out_specs=(P("col"), P("row")), check_vma=False
    )
```

```python
import jax
import jax.numpy as jnp
from jax import lax
from jax.sharding import PartitionSpec as P

RUIZ = 2
ITERS = 2


EPSILON = 1e-06
HIGHEST = lax.Precision.HIGHEST
HIGH = lax.Precision.HIGH


def butterfly(value, axis, size, combine):
    bit = 1
    while bit < size:
        pairs = [(i, i ^ bit) for i in range(size)]
        value = combine(value, lax.ppermute(value, axis, pairs))
        bit *= 2
    return value


def exchange(value, axis, size, reduce):
    spread = jnp.broadcast_to(value[None], (size,) + value.shape)
    return reduce(lax.all_to_all(spread, axis, 0, 0, tiled=False), axis=0)


def _max(a, b):
    return jax.tree.map(jnp.maximum, a, b)


def _add(a, b):
    return jax.tree.map(jnp.add, a, b)


def make_local(n_row, n_col):
    def local(
        tile_values,
        tile_coords,
        tile_count,
        objective,
        lower,
        upper,
        rhs,
        primal_start,
        dual_start,
        step_size,
    ):
        tile_width = tile_values.shape[-1]
        slot_count = tile_values.shape[2]
        matrix = tile_values.reshape(slot_count, tile_width, tile_width)
        coords = tile_coords.reshape(slot_count, 2)
        block_rows = coords[:, 0]
        block_cols = coords[:, 1]
        row_blocks = rhs.shape[0] // tile_width
        col_blocks = objective.shape[0] // tile_width
        link_start = col_blocks * (n_col // n_row)
        r = lax.axis_index("row")
        c = lax.axis_index("col")
        is_period = (c % n_row) == r
        seg_start = (c // n_row) * col_blocks
        row_ids = jnp.arange(row_blocks, dtype=jnp.int32)[:, None]
        own_period = is_period & (row_ids >= seg_start) & (row_ids < seg_start + col_blocks)

        in_use = (jnp.arange(slot_count, dtype=jnp.int32) < tile_count.reshape(())).astype(jnp.float32)
        row_onehot = (jnp.arange(row_blocks, dtype=jnp.int32)[:, None] == block_rows[None, :]).astype(
            jnp.float32
        ) * in_use[None, :]
        col_onehot = (jnp.arange(col_blocks, dtype=jnp.int32)[:, None] == block_cols[None, :]).astype(
            jnp.float32
        ) * in_use[None, :]
        magnitude = jnp.abs(matrix) * in_use[:, None, None]

        def row_peaks(col_scale):
            col_pieces = jnp.take(col_scale, block_cols, axis=0)
            row_local = jnp.max(magnitude * col_pieces[:, None, :], axis=2)
            return jnp.zeros((row_blocks, tile_width), jnp.float32).at[block_rows].max(row_local)

        def col_peaks(row_scale):
            row_pieces = jnp.take(row_scale, block_rows, axis=0)
            col_local = jnp.max(magnitude * row_pieces[:, :, None], axis=1)
            return jnp.zeros((col_blocks, tile_width), jnp.float32).at[block_cols].max(col_local)

        def rescale(scale, peak):
            return scale / jnp.sqrt(scale * peak + EPSILON)

        rhs_b = rhs.reshape(row_blocks, tile_width)
        obj_b = objective.reshape(col_blocks, tile_width)
        lanes = jnp.arange(tile_width, dtype=jnp.int32)[None, :]

        row_scale0 = jnp.ones((row_blocks, tile_width), jnp.float32)
        col_scale0 = jnp.ones((col_blocks, tile_width), jnp.float32)
        row_local1 = row_peaks(col_scale0)
        link_peak1 = exchange(row_local1[link_start:], "col", n_col, jnp.max)
        row_scale1 = rescale(row_scale0, jnp.concatenate([row_local1[:link_start], link_peak1], axis=0))
        col_local1 = col_peaks(row_scale0)
        col_local2 = col_peaks(row_scale1)
        col_both = butterfly(jnp.concatenate([col_local1, col_local2], axis=0), "row", n_row, _max)
        col_scale1 = rescale(col_scale0, col_both[:col_blocks])
        col_scale = rescale(col_scale1, col_both[col_blocks:])

        row_local2 = row_peaks(col_scale1)
        own_scale2 = rescale(row_scale1, row_local2)
        own_bound = own_scale2 * rhs_b
        period_square = jnp.sum(jnp.where(own_period, own_bound * own_bound, 0.0))
        cost = col_scale * obj_b
        cost_square = jnp.sum(cost * cost)
        slot = jnp.where(lanes == c, cost_square, 0.0)
        slot = jnp.where(is_period & (lanes == n_col + c // n_row), period_square, slot)
        packed2 = exchange(jnp.concatenate([row_local2[link_start:], slot], axis=0), "col", n_col, jnp.max)
        link_peak2 = packed2[: row_blocks - link_start]
        spare = packed2[row_blocks - link_start]
        cost_total = jnp.sum(spare[:n_col]).reshape(1)
        period_total = jnp.sum(spare[n_col : n_col + n_col // n_row]).reshape(1)
        row_scale = rescale(row_scale1, jnp.concatenate([row_local2[:link_start], link_peak2], axis=0))

        bound = row_scale * rhs_b
        low_scaled = lower.reshape(col_blocks, tile_width) / col_scale
        high_scaled = upper.reshape(col_blocks, tile_width) / col_scale
        primal = primal_start.reshape(col_blocks, tile_width) / col_scale
        dual = dual_start.reshape(row_blocks, tile_width) / row_scale
        link_bound = bound[link_start:]
        bound_part = period_total + jnp.sum(link_bound * link_bound).reshape(1)

        def adjoint_local(dual):
            pieces = jnp.take(row_scale * dual, block_rows, axis=0)
            products = jnp.einsum("tij,ti->tj", matrix, pieces, precision=HIGH)
            return jnp.dot(col_onehot, products, precision=HIGHEST)

        def forward_local(extra):
            forward_pieces = jnp.take(col_scale * extra, block_cols, axis=0)
            forward_products = jnp.sum(matrix * forward_pieces[:, None, :], axis=2)
            return jnp.dot(row_onehot, forward_products, precision=HIGHEST)

        image0_part = adjoint_local(dual)
        bound_row = jnp.where(lanes == 0, bound_part[0], 0.0)
        packed3 = exchange(jnp.concatenate([image0_part, bound_row], axis=0), "row", n_row, jnp.sum)
        image = packed3[:col_blocks]
        bound_total = packed3[col_blocks, :1]
        weight = jnp.sqrt(cost_total[0] + EPSILON) / jnp.sqrt(bound_total[0] + EPSILON)
        primal_step = step_size[0] / weight
        dual_step = step_size[0] * weight

        for iteration in range(ITERS):
            if iteration > 0:
                image = exchange(adjoint_local(dual), "row", n_row, jnp.sum)
            moved = jnp.clip(primal - primal_step * (cost - col_scale * image), low_scaled, high_scaled)
            extra = 2.0 * moved - primal
            partial_rows = forward_local(extra)
            primal = moved
            if iteration < ITERS - 1:
                link_total = exchange(partial_rows[link_start:], "col", n_col, jnp.sum)
                total = jnp.concatenate([partial_rows[:link_start], link_total], axis=0)
                dual = jnp.maximum(dual + dual_step * (bound - row_scale * total), 0.0)
            else:
                own_dual = jnp.maximum(dual + dual_step * (bound - row_scale * partial_rows), 0.0)
                own_out = jnp.where(own_period, row_scale * own_dual, 0.0)
                segment = lax.dynamic_slice_in_dim(own_out, seg_start, col_blocks, axis=0)
                carried = jnp.concatenate([segment, partial_rows[link_start:]], axis=0)
                bit = 1
                while bit < n_row:
                    carried = carried + lax.ppermute(carried, "col", [(i, i ^ bit) for i in range(n_col)])
                    bit *= 2
                segments = carried[:col_blocks]
                link_sum = carried[col_blocks:]
                group = c // n_row
                while bit < n_col:
                    held = segments.shape[0]
                    other = lax.ppermute(
                        jnp.concatenate([segments, link_sum], axis=0), "col", [(i, i ^ bit) for i in range(n_col)]
                    )
                    upper_half = (group & (bit // n_row)) != 0
                    segments = jnp.where(
                        upper_half,
                        jnp.concatenate([other[:held], segments], axis=0),
                        jnp.concatenate([segments, other[:held]], axis=0),
                    )
                    link_sum = link_sum + other[held:]
                    bit *= 2
                joined = jnp.concatenate([segments, link_sum], axis=0)
                link_dual = jnp.maximum(
                    dual[link_start:]
                    + dual_step * (bound[link_start:] - row_scale[link_start:] * joined[link_start:]),
                    0.0,
                )
                dual_out = jnp.concatenate([joined[:link_start], row_scale[link_start:] * link_dual], axis=0)
        return ((col_scale * primal).reshape(-1), dual_out.reshape(-1))

    return local


def solution(mesh):
    placed = (
        P("row", "col", None, None, None),
        P("row", "col", None, None),
        P("row", "col"),
        P("col"),
        P("col"),
        P("col"),
        P("row"),
        P("col"),
        P("row"),
        P(),
    )
    local = make_local(mesh.shape["row"], mesh.shape["col"])
    return jax.shard_map(
        local, mesh=mesh, in_specs=placed, out_specs=(P("col"), P("row")), check_vma=False
    )
```

```python
import jax
import jax.numpy as jnp
from jax import lax
from jax.sharding import PartitionSpec as P

RUIZ = 2
ITERS = 2


EPSILON = 1e-06
HIGHEST = lax.Precision.HIGHEST
HIGH = lax.Precision.HIGH


def butterfly(value, axis, size, combine):
    bit = 1
    while bit < size:
        pairs = [(i, i ^ bit) for i in range(size)]
        value = combine(value, lax.ppermute(value, axis, pairs))
        bit *= 2
    return value


def exchange(value, axis, size, reduce):
    spread = jnp.broadcast_to(value[None], (size,) + value.shape)
    return reduce(lax.all_to_all(spread, axis, 0, 0, tiled=False), axis=0)


def _max(a, b):
    return jax.tree.map(jnp.maximum, a, b)


def _add(a, b):
    return jax.tree.map(jnp.add, a, b)


def make_local(n_row, n_col):
    def local(
        tile_values,
        tile_coords,
        tile_count,
        objective,
        lower,
        upper,
        rhs,
        primal_start,
        dual_start,
        step_size,
    ):
        tile_width = tile_values.shape[-1]
        slot_count = tile_values.shape[2]
        matrix = tile_values.reshape(slot_count, tile_width, tile_width)
        coords = tile_coords.reshape(slot_count, 2)
        block_rows = coords[:, 0]
        block_cols = coords[:, 1]
        row_blocks = rhs.shape[0] // tile_width
        col_blocks = objective.shape[0] // tile_width
        link_start = col_blocks * (n_col // n_row)
        r = lax.axis_index("row")
        c = lax.axis_index("col")
        is_period = (c % n_row) == r
        seg_start = (c // n_row) * col_blocks
        row_ids = jnp.arange(row_blocks, dtype=jnp.int32)[:, None]
        own_period = is_period & (row_ids >= seg_start) & (row_ids < seg_start + col_blocks)

        in_use = (jnp.arange(slot_count, dtype=jnp.int32) < tile_count.reshape(())).astype(jnp.float32)
        row_onehot = (jnp.arange(row_blocks, dtype=jnp.int32)[:, None] == block_rows[None, :]).astype(
            jnp.float32
        ) * in_use[None, :]
        col_onehot = (jnp.arange(col_blocks, dtype=jnp.int32)[:, None] == block_cols[None, :]).astype(
            jnp.float32
        ) * in_use[None, :]
        magnitude = jnp.abs(matrix) * in_use[:, None, None]

        def row_peaks(col_scale):
            col_pieces = jnp.take(col_scale, block_cols, axis=0)
            row_local = jnp.max(magnitude * col_pieces[:, None, :], axis=2)
            return jnp.zeros((row_blocks, tile_width), jnp.float32).at[block_rows].max(row_local)

        def col_peaks(row_scale):
            row_pieces = jnp.take(row_scale, block_rows, axis=0)
            col_local = jnp.max(magnitude * row_pieces[:, :, None], axis=1)
            return jnp.zeros((col_blocks, tile_width), jnp.float32).at[block_cols].max(col_local)

        def rescale(scale, peak):
            return scale / jnp.sqrt(scale * peak + EPSILON)

        rhs_b = rhs.reshape(row_blocks, tile_width)
        obj_b = objective.reshape(col_blocks, tile_width)
        lanes = jnp.arange(tile_width, dtype=jnp.int32)[None, :]

        row_scale0 = jnp.ones((row_blocks, tile_width), jnp.float32)
        col_scale0 = jnp.ones((col_blocks, tile_width), jnp.float32)
        row_local1 = row_peaks(col_scale0)
        link_peak1 = exchange(row_local1[link_start:], "col", n_col, jnp.max)
        row_scale1 = rescale(row_scale0, jnp.concatenate([row_local1[:link_start], link_peak1], axis=0))
        col_local1 = col_peaks(row_scale0)
        col_local2 = col_peaks(row_scale1)
        first_pieces = jnp.take(dual_start.reshape(row_blocks, tile_width), block_rows, axis=0)
        first_products = jnp.einsum("tij,ti->tj", matrix, first_pieces, precision=HIGH)
        image0_part = jnp.dot(col_onehot, first_products, precision=HIGHEST)
        peak_rows = 2 * col_blocks

        def max_then_add(a, b):
            return jnp.concatenate([jnp.maximum(a[:peak_rows], b[:peak_rows]), a[peak_rows:] + b[peak_rows:]], axis=0)

        col_both = butterfly(
            jnp.concatenate([col_local1, col_local2, image0_part], axis=0), "row", n_row, max_then_add
        )
        col_scale1 = rescale(col_scale0, col_both[:col_blocks])
        col_scale = rescale(col_scale1, col_both[col_blocks:peak_rows])
        image = col_both[peak_rows:]

        row_local2 = row_peaks(col_scale1)
        own_scale2 = rescale(row_scale1, row_local2)
        own_bound = own_scale2 * rhs_b
        period_square = jnp.sum(jnp.where(own_period, own_bound * own_bound, 0.0))
        cost = col_scale * obj_b
        cost_square = jnp.sum(cost * cost)
        slot = jnp.where(lanes == c, cost_square, 0.0)
        slot = jnp.where(is_period & (lanes == n_col + c // n_row), period_square, slot)
        packed2 = exchange(jnp.concatenate([row_local2[link_start:], slot], axis=0), "col", n_col, jnp.max)
        link_peak2 = packed2[: row_blocks - link_start]
        spare = packed2[row_blocks - link_start]
        cost_total = jnp.sum(spare[:n_col]).reshape(1)
        period_total = jnp.sum(spare[n_col : n_col + n_col // n_row]).reshape(1)
        row_scale = rescale(row_scale1, jnp.concatenate([row_local2[:link_start], link_peak2], axis=0))

        bound = row_scale * rhs_b
        low_scaled = lower.reshape(col_blocks, tile_width) / col_scale
        high_scaled = upper.reshape(col_blocks, tile_width) / col_scale
        primal = primal_start.reshape(col_blocks, tile_width) / col_scale
        dual = dual_start.reshape(row_blocks, tile_width) / row_scale
        link_bound = bound[link_start:]
        bound_part = period_total + jnp.sum(link_bound * link_bound).reshape(1)

        def adjoint_local(dual):
            pieces = jnp.take(row_scale * dual, block_rows, axis=0)
            products = jnp.einsum("tij,ti->tj", matrix, pieces, precision=HIGH)
            return jnp.dot(col_onehot, products, precision=HIGHEST)

        def forward_local(extra):
            forward_pieces = jnp.take(col_scale * extra, block_cols, axis=0)
            forward_products = jnp.sum(matrix * forward_pieces[:, None, :], axis=2)
            return jnp.dot(row_onehot, forward_products, precision=HIGHEST)

        bound_row = jnp.where(lanes == 0, bound_part[0], 0.0)
        bound_total = exchange(bound_row, "row", n_row, jnp.sum)[0, :1]
        weight = jnp.sqrt(cost_total[0] + EPSILON) / jnp.sqrt(bound_total[0] + EPSILON)
        primal_step = step_size[0] / weight
        dual_step = step_size[0] * weight

        for iteration in range(ITERS):
            if iteration > 0:
                image = exchange(adjoint_local(dual), "row", n_row, jnp.sum)
            moved = jnp.clip(primal - primal_step * (cost - col_scale * image), low_scaled, high_scaled)
            extra = 2.0 * moved - primal
            partial_rows = forward_local(extra)
            primal = moved
            if iteration < ITERS - 1:
                link_total = exchange(partial_rows[link_start:], "col", n_col, jnp.sum)
                total = jnp.concatenate([partial_rows[:link_start], link_total], axis=0)
                dual = jnp.maximum(dual + dual_step * (bound - row_scale * total), 0.0)
            else:
                own_dual = jnp.maximum(dual + dual_step * (bound - row_scale * partial_rows), 0.0)
                own_out = jnp.where(own_period, row_scale * own_dual, 0.0)
                segment = lax.dynamic_slice_in_dim(own_out, seg_start, col_blocks, axis=0)
                carried = jnp.concatenate([segment, partial_rows[link_start:]], axis=0)
                bit = 1
                while bit < n_row:
                    carried = carried + lax.ppermute(carried, "col", [(i, i ^ bit) for i in range(n_col)])
                    bit *= 2
                segments = carried[:col_blocks]
                link_sum = carried[col_blocks:]
                group = c // n_row
                while bit < n_col:
                    held = segments.shape[0]
                    other = lax.ppermute(
                        jnp.concatenate([segments, link_sum], axis=0), "col", [(i, i ^ bit) for i in range(n_col)]
                    )
                    upper_half = (group & (bit // n_row)) != 0
                    segments = jnp.where(
                        upper_half,
                        jnp.concatenate([other[:held], segments], axis=0),
                        jnp.concatenate([segments, other[:held]], axis=0),
                    )
                    link_sum = link_sum + other[held:]
                    bit *= 2
                joined = jnp.concatenate([segments, link_sum], axis=0)
                link_dual = jnp.maximum(
                    dual[link_start:]
                    + dual_step * (bound[link_start:] - row_scale[link_start:] * joined[link_start:]),
                    0.0,
                )
                dual_out = jnp.concatenate([joined[:link_start], row_scale[link_start:] * link_dual], axis=0)
        return ((col_scale * primal).reshape(-1), dual_out.reshape(-1))

    return local


def solution(mesh):
    placed = (
        P("row", "col", None, None, None),
        P("row", "col", None, None),
        P("row", "col"),
        P("col"),
        P("col"),
        P("col"),
        P("row"),
        P("col"),
        P("row"),
        P(),
    )
    local = make_local(mesh.shape["row"], mesh.shape["col"])
    return jax.shard_map(
        local, mesh=mesh, in_specs=placed, out_specs=(P("col"), P("row")), check_vma=False
    )
```

```python
import jax
import jax.numpy as jnp
from jax import lax
from jax.sharding import PartitionSpec as P

RUIZ = 2
ITERS = 2


EPSILON = 1e-06
HIGHEST = lax.Precision.HIGHEST
HIGH = lax.Precision.HIGH


def butterfly(value, axis, size, combine):
    bit = 1
    while bit < size:
        pairs = [(i, i ^ bit) for i in range(size)]
        value = combine(value, lax.ppermute(value, axis, pairs))
        bit *= 2
    return value


def exchange(value, axis, size, reduce):
    spread = jnp.broadcast_to(value[None], (size,) + value.shape)
    return reduce(lax.all_to_all(spread, axis, 0, 0, tiled=False), axis=0)


def _max(a, b):
    return jax.tree.map(jnp.maximum, a, b)


def _add(a, b):
    return jax.tree.map(jnp.add, a, b)


def make_local(n_row, n_col):
    def local(
        tile_values,
        tile_coords,
        tile_count,
        objective,
        lower,
        upper,
        rhs,
        primal_start,
        dual_start,
        step_size,
    ):
        tile_width = tile_values.shape[-1]
        slot_count = tile_values.shape[2]
        matrix = tile_values.reshape(slot_count, tile_width, tile_width)
        coords = tile_coords.reshape(slot_count, 2)
        block_rows = coords[:, 0]
        block_cols = coords[:, 1]
        row_blocks = rhs.shape[0] // tile_width
        col_blocks = objective.shape[0] // tile_width
        link_start = col_blocks * (n_col // n_row)
        r = lax.axis_index("row")
        c = lax.axis_index("col")
        is_period = (c % n_row) == r
        seg_start = (c // n_row) * col_blocks
        row_ids = jnp.arange(row_blocks, dtype=jnp.int32)[:, None]
        own_period = is_period & (row_ids >= seg_start) & (row_ids < seg_start + col_blocks)

        in_use = (jnp.arange(slot_count, dtype=jnp.int32) < tile_count.reshape(())).astype(jnp.float32)
        row_onehot = (jnp.arange(row_blocks, dtype=jnp.int32)[:, None] == block_rows[None, :]).astype(
            jnp.float32
        ) * in_use[None, :]
        col_onehot = (jnp.arange(col_blocks, dtype=jnp.int32)[:, None] == block_cols[None, :]).astype(
            jnp.float32
        ) * in_use[None, :]
        magnitude = jnp.abs(matrix) * in_use[:, None, None]

        def row_peaks(col_scale):
            col_pieces = jnp.take(col_scale, block_cols, axis=0)
            row_local = jnp.max(magnitude * col_pieces[:, None, :], axis=2)
            return jnp.zeros((row_blocks, tile_width), jnp.float32).at[block_rows].max(row_local)

        def col_peaks(row_scale):
            row_pieces = jnp.take(row_scale, block_rows, axis=0)
            col_local = jnp.max(magnitude * row_pieces[:, :, None], axis=1)
            return jnp.zeros((col_blocks, tile_width), jnp.float32).at[block_cols].max(col_local)

        def rescale(scale, peak):
            return scale / jnp.sqrt(scale * peak + EPSILON)

        rhs_b = rhs.reshape(row_blocks, tile_width)
        obj_b = objective.reshape(col_blocks, tile_width)
        lanes = jnp.arange(tile_width, dtype=jnp.int32)[None, :]

        row_scale0 = jnp.ones((row_blocks, tile_width), jnp.float32)
        col_scale0 = jnp.ones((col_blocks, tile_width), jnp.float32)
        row_local1 = row_peaks(col_scale0)
        link_peak1 = exchange(row_local1[link_start:], "col", n_col, jnp.max)
        row_scale1 = rescale(row_scale0, jnp.concatenate([row_local1[:link_start], link_peak1], axis=0))
        col_local1 = col_peaks(row_scale0)
        col_local2 = col_peaks(row_scale1)
        first_pieces = jnp.take(dual_start.reshape(row_blocks, tile_width), block_rows, axis=0)
        first_products = jnp.sum(matrix * first_pieces[:, :, None], axis=1)
        image0_part = jnp.dot(col_onehot, first_products, precision=HIGHEST)
        peak_rows = 2 * col_blocks

        def max_then_add(a, b):
            return jnp.concatenate([jnp.maximum(a[:peak_rows], b[:peak_rows]), a[peak_rows:] + b[peak_rows:]], axis=0)

        col_both = butterfly(
            jnp.concatenate([col_local1, col_local2, image0_part], axis=0), "row", n_row, max_then_add
        )
        col_scale1 = rescale(col_scale0, col_both[:col_blocks])
        col_scale = rescale(col_scale1, col_both[col_blocks:peak_rows])
        image = col_both[peak_rows:]

        row_local2 = row_peaks(col_scale1)
        own_scale2 = rescale(row_scale1, row_local2)
        own_bound = own_scale2 * rhs_b
        period_square = jnp.sum(jnp.where(own_period, own_bound * own_bound, 0.0))
        cost = col_scale * obj_b
        cost_square = jnp.sum(cost * cost)
        slot = jnp.where(lanes == c, cost_square, 0.0)
        slot = jnp.where(is_period & (lanes == n_col + c // n_row), period_square, slot)
        packed2 = exchange(jnp.concatenate([row_local2[link_start:], slot], axis=0), "col", n_col, jnp.max)
        link_peak2 = packed2[: row_blocks - link_start]
        spare = packed2[row_blocks - link_start]
        cost_total = jnp.sum(spare[:n_col]).reshape(1)
        period_total = jnp.sum(spare[n_col : n_col + n_col // n_row]).reshape(1)
        row_scale = rescale(row_scale1, jnp.concatenate([row_local2[:link_start], link_peak2], axis=0))

        bound = row_scale * rhs_b
        low_scaled = lower.reshape(col_blocks, tile_width) / col_scale
        high_scaled = upper.reshape(col_blocks, tile_width) / col_scale
        primal = primal_start.reshape(col_blocks, tile_width) / col_scale
        dual = dual_start.reshape(row_blocks, tile_width) / row_scale
        link_bound = bound[link_start:]
        bound_part = period_total + jnp.sum(link_bound * link_bound).reshape(1)

        def adjoint_local(dual):
            pieces = jnp.take(row_scale * dual, block_rows, axis=0)
            products = jnp.einsum("tij,ti->tj", matrix, pieces, precision=HIGH)
            return jnp.dot(col_onehot, products, precision=HIGHEST)

        def forward_local(extra):
            forward_pieces = jnp.take(col_scale * extra, block_cols, axis=0)
            forward_products = jnp.sum(matrix * forward_pieces[:, None, :], axis=2)
            return jnp.dot(row_onehot, forward_products, precision=HIGHEST)

        bound_row = jnp.where(lanes == 0, bound_part[0], 0.0)
        bound_total = exchange(bound_row, "row", n_row, jnp.sum)[0, :1]
        weight = jnp.sqrt(cost_total[0] + EPSILON) / jnp.sqrt(bound_total[0] + EPSILON)
        primal_step = step_size[0] / weight
        dual_step = step_size[0] * weight

        for iteration in range(ITERS):
            if iteration > 0:
                image = exchange(adjoint_local(dual), "row", n_row, jnp.sum)
            moved = jnp.clip(primal - primal_step * (cost - col_scale * image), low_scaled, high_scaled)
            extra = 2.0 * moved - primal
            partial_rows = forward_local(extra)
            primal = moved
            if iteration < ITERS - 1:
                link_total = exchange(partial_rows[link_start:], "col", n_col, jnp.sum)
                total = jnp.concatenate([partial_rows[:link_start], link_total], axis=0)
                dual = jnp.maximum(dual + dual_step * (bound - row_scale * total), 0.0)
            else:
                own_dual = jnp.maximum(dual + dual_step * (bound - row_scale * partial_rows), 0.0)
                own_out = jnp.where(own_period, row_scale * own_dual, 0.0)
                segment = lax.dynamic_slice_in_dim(own_out, seg_start, col_blocks, axis=0)
                carried = jnp.concatenate([segment, partial_rows[link_start:]], axis=0)
                bit = 1
                while bit < n_row:
                    carried = carried + lax.ppermute(carried, "col", [(i, i ^ bit) for i in range(n_col)])
                    bit *= 2
                segments = carried[:col_blocks]
                link_sum = carried[col_blocks:]
                group = c // n_row
                while bit < n_col:
                    held = segments.shape[0]
                    other = lax.ppermute(
                        jnp.concatenate([segments, link_sum], axis=0), "col", [(i, i ^ bit) for i in range(n_col)]
                    )
                    upper_half = (group & (bit // n_row)) != 0
                    segments = jnp.where(
                        upper_half,
                        jnp.concatenate([other[:held], segments], axis=0),
                        jnp.concatenate([segments, other[:held]], axis=0),
                    )
                    link_sum = link_sum + other[held:]
                    bit *= 2
                joined = jnp.concatenate([segments, link_sum], axis=0)
                link_dual = jnp.maximum(
                    dual[link_start:]
                    + dual_step * (bound[link_start:] - row_scale[link_start:] * joined[link_start:]),
                    0.0,
                )
                dual_out = jnp.concatenate([joined[:link_start], row_scale[link_start:] * link_dual], axis=0)
        return ((col_scale * primal).reshape(-1), dual_out.reshape(-1))

    return local


def solution(mesh):
    placed = (
        P("row", "col", None, None, None),
        P("row", "col", None, None),
        P("row", "col"),
        P("col"),
        P("col"),
        P("col"),
        P("row"),
        P("col"),
        P("row"),
        P(),
    )
    local = make_local(mesh.shape["row"], mesh.shape["col"])
    return jax.shard_map(
        local, mesh=mesh, in_specs=placed, out_specs=(P("col"), P("row")), check_vma=False
    )
```

```python
import jax
import jax.numpy as jnp
from jax import lax
from jax.sharding import PartitionSpec as P

RUIZ = 2
ITERS = 2


EPSILON = 1e-06
HIGHEST = lax.Precision.HIGHEST
HIGH = lax.Precision.HIGH


def butterfly(value, axis, size, combine):
    bit = 1
    while bit < size:
        pairs = [(i, i ^ bit) for i in range(size)]
        value = combine(value, lax.ppermute(value, axis, pairs))
        bit *= 2
    return value


def exchange(value, axis, size, reduce):
    spread = jnp.broadcast_to(value[None], (size,) + value.shape)
    return reduce(lax.all_to_all(spread, axis, 0, 0, tiled=False), axis=0)


def _max(a, b):
    return jax.tree.map(jnp.maximum, a, b)


def _add(a, b):
    return jax.tree.map(jnp.add, a, b)


def make_local(n_row, n_col):
    def local(
        tile_values,
        tile_coords,
        tile_count,
        objective,
        lower,
        upper,
        rhs,
        primal_start,
        dual_start,
        step_size,
    ):
        tile_width = tile_values.shape[-1]
        slot_count = tile_values.shape[2]
        matrix = tile_values.reshape(slot_count, tile_width, tile_width)
        coords = tile_coords.reshape(slot_count, 2)
        block_rows = coords[:, 0]
        block_cols = coords[:, 1]
        row_blocks = rhs.shape[0] // tile_width
        col_blocks = objective.shape[0] // tile_width
        link_start = col_blocks * (n_col // n_row)
        r = lax.axis_index("row")
        c = lax.axis_index("col")
        is_period = (c % n_row) == r
        seg_start = (c // n_row) * col_blocks
        row_ids = jnp.arange(row_blocks, dtype=jnp.int32)[:, None]
        own_period = is_period & (row_ids >= seg_start) & (row_ids < seg_start + col_blocks)

        in_use = (jnp.arange(slot_count, dtype=jnp.int32) < tile_count.reshape(())).astype(jnp.float32)
        row_onehot = (jnp.arange(row_blocks, dtype=jnp.int32)[:, None] == block_rows[None, :]).astype(
            jnp.float32
        ) * in_use[None, :]
        col_onehot = (jnp.arange(col_blocks, dtype=jnp.int32)[:, None] == block_cols[None, :]).astype(
            jnp.float32
        ) * in_use[None, :]
        magnitude = jnp.abs(matrix) * in_use[:, None, None]

        def row_peaks(col_scale):
            col_pieces = jnp.take(col_scale, block_cols, axis=0)
            row_local = jnp.max(magnitude * col_pieces[:, None, :], axis=2)
            return jnp.zeros((row_blocks, tile_width), jnp.float32).at[block_rows].max(row_local)

        def col_peaks(row_scale):
            row_pieces = jnp.take(row_scale, block_rows, axis=0)
            col_local = jnp.max(magnitude * row_pieces[:, :, None], axis=1)
            return jnp.zeros((col_blocks, tile_width), jnp.float32).at[block_cols].max(col_local)

        def rescale(scale, peak):
            return scale / jnp.sqrt(scale * peak + EPSILON)

        rhs_b = rhs.reshape(row_blocks, tile_width)
        obj_b = objective.reshape(col_blocks, tile_width)
        lanes = jnp.arange(tile_width, dtype=jnp.int32)[None, :]

        row_scale0 = jnp.ones((row_blocks, tile_width), jnp.float32)
        col_scale0 = jnp.ones((col_blocks, tile_width), jnp.float32)
        row_local1 = row_peaks(col_scale0)
        link_peak1 = exchange(row_local1[link_start:], "col", n_col, jnp.max)
        row_scale1 = rescale(row_scale0, jnp.concatenate([row_local1[:link_start], link_peak1], axis=0))
        col_local1 = col_peaks(row_scale0)
        col_local2 = col_peaks(row_scale1)
        first_pieces = jnp.take(dual_start.reshape(row_blocks, tile_width), block_rows, axis=0)
        first_products = jnp.sum(matrix * first_pieces[:, :, None], axis=1)
        image0_part = jnp.dot(col_onehot, first_products, precision=HIGHEST)
        peak_rows = 2 * col_blocks

        def max_then_add(a, b):
            return jnp.concatenate([jnp.maximum(a[:peak_rows], b[:peak_rows]), a[peak_rows:] + b[peak_rows:]], axis=0)

        col_both = butterfly(
            jnp.concatenate([col_local1, col_local2, image0_part], axis=0), "row", n_row, max_then_add
        )
        col_scale1 = rescale(col_scale0, col_both[:col_blocks])
        col_scale = rescale(col_scale1, col_both[col_blocks:peak_rows])
        image = col_both[peak_rows:]

        row_local2 = row_peaks(col_scale1)
        own_scale2 = rescale(row_scale1, row_local2)
        own_bound = own_scale2 * rhs_b
        period_square = jnp.sum(jnp.where(own_period, own_bound * own_bound, 0.0))
        cost = col_scale * obj_b
        cost_square = jnp.sum(cost * cost)
        slot = jnp.where(lanes == c, cost_square, 0.0)
        slot = jnp.where(is_period & (lanes == n_col + c // n_row), period_square, slot)
        packed2 = exchange(jnp.concatenate([row_local2[link_start:], slot], axis=0), "col", n_col, jnp.max)
        link_peak2 = packed2[: row_blocks - link_start]
        spare = packed2[row_blocks - link_start]
        cost_total = jnp.sum(spare[:n_col]).reshape(1)
        period_total = jnp.sum(spare[n_col : n_col + n_col // n_row]).reshape(1)
        row_scale = rescale(row_scale1, jnp.concatenate([row_local2[:link_start], link_peak2], axis=0))

        bound = row_scale * rhs_b
        low_scaled = lower.reshape(col_blocks, tile_width) / col_scale
        high_scaled = upper.reshape(col_blocks, tile_width) / col_scale
        primal = primal_start.reshape(col_blocks, tile_width) / col_scale
        dual = dual_start.reshape(row_blocks, tile_width) / row_scale
        link_bound = bound[link_start:]
        bound_part = period_total + jnp.sum(link_bound * link_bound).reshape(1)

        def adjoint_local(dual):
            pieces = jnp.take(row_scale * dual, block_rows, axis=0)
            products = jnp.einsum("tij,ti->tj", matrix, pieces, precision=HIGH)
            return jnp.dot(col_onehot, products, precision=HIGHEST)

        def forward_local(extra):
            forward_pieces = jnp.take(col_scale * extra, block_cols, axis=0)
            forward_products = jnp.sum(matrix * forward_pieces[:, None, :], axis=2)
            return jnp.dot(row_onehot, forward_products, precision=HIGHEST)

        bound_row = jnp.where(lanes == 0, bound_part[0], 0.0)
        bound_total = exchange(bound_row, "row", n_row, jnp.sum)[0, :1]
        weight = jnp.sqrt(cost_total[0] + EPSILON) / jnp.sqrt(bound_total[0] + EPSILON)
        primal_step = step_size[0] / weight
        dual_step = step_size[0] * weight

        for iteration in range(ITERS):
            if iteration > 0:
                image = exchange(adjoint_local(dual), "row", n_row, jnp.sum)
            moved = jnp.clip(primal - primal_step * (cost - col_scale * image), low_scaled, high_scaled)
            extra = 2.0 * moved - primal
            partial_rows = forward_local(extra)
            primal = moved
            if iteration < ITERS - 1:
                link_total = exchange(partial_rows[link_start:], "col", n_col, jnp.sum)
                total = jnp.concatenate([partial_rows[:link_start], link_total], axis=0)
                dual = jnp.maximum(dual + dual_step * (bound - row_scale * total), 0.0)
            else:
                own_dual = jnp.maximum(dual + dual_step * (bound - row_scale * partial_rows), 0.0)
                own_out = jnp.where(own_period, row_scale * own_dual, 0.0)
                segment = lax.dynamic_slice_in_dim(own_out, seg_start, col_blocks, axis=0)
                carried = jnp.concatenate([segment, partial_rows[link_start:]], axis=0)
                spread = jnp.broadcast_to(carried[None], (n_col,) + carried.shape)
                received = lax.all_to_all(spread, "col", 0, 0, tiled=False)
                link_sum = jnp.sum(received[:, col_blocks:], axis=0)
                owners = r + n_row * jnp.arange(n_col // n_row, dtype=jnp.int32)
                segments = jnp.take(received[:, :col_blocks], owners, axis=0).reshape(link_start, tile_width)
                joined = jnp.concatenate([segments, link_sum], axis=0)
                link_dual = jnp.maximum(
                    dual[link_start:]
                    + dual_step * (bound[link_start:] - row_scale[link_start:] * joined[link_start:]),
                    0.0,
                )
                dual_out = jnp.concatenate([joined[:link_start], row_scale[link_start:] * link_dual], axis=0)
        return ((col_scale * primal).reshape(-1), dual_out.reshape(-1))

    return local


def solution(mesh):
    placed = (
        P("row", "col", None, None, None),
        P("row", "col", None, None),
        P("row", "col"),
        P("col"),
        P("col"),
        P("col"),
        P("row"),
        P("col"),
        P("row"),
        P(),
    )
    local = make_local(mesh.shape["row"], mesh.shape["col"])
    return jax.shard_map(
        local, mesh=mesh, in_specs=placed, out_specs=(P("col"), P("row")), check_vma=False
    )
```
